256 devices in a mesh: seq: 32 (over z, x_hi, core), fsdp: 8 (over x_lo, y).
Axes of the slice: x: 4 (x_hi: 2, x_lo: 2; x = x_hi * 2 + x_lo), y: 4, z: 8, core: 2. Of those that a mesh axis runs over, the one named last changes fastest.
Arguments:
- text_states: bfloat16 [8192, 8192], P('seq'), may hold values from -6 to 6
- images: bfloat16 [32, 1601, 8192], P('seq', None, 'fsdp'), may hold values from -6 to 6
- norm_gain: float32 [8192], replicated, may hold values from 0.1 to 1.9
- query_weight: bfloat16 [8192, 4096], P('seq', 'fsdp'), may hold values from -0.0625 to 0.0625
- image_projection_weight: bfloat16 [8192, 2048], P(('fsdp', 'seq')), may hold values from -0.0625 to 0.0625
- query_gain: float32 [128], replicated, may hold values from 0.5 to 2
- key_gain: float32 [128], replicated, may hold values from 0.5 to 2
- admission: int32 [32, 32], P('seq'), may hold values from 0 to 1, as said below
Outputs:
- attended: bfloat16 [8192, 4096], P('seq', 'fsdp')
The draws below stay inside these ranges and needn't reach their ends.
Inputs may be any that keep to these rules, and one draw needn't show every extreme that they name: admission[c, m] is 1 for m = c and for at most 2 of the images m with c - 4 <= m < c, and 0 elsewhere; in every draw some text blocks, the last one among them, attend to exactly 3 images.
All inputs are finite; a program needn't handle non-finite values.
Results may differ from the reference program's by a relative error of at most 0.035.
Values may be sent and summed in bfloat16 or wider, within the bound.
No kernel may reach another device: no remote copies, remote signals or barrier semaphores. Data moves between devices by JAX's collectives and lax.ppermute only.
A program may use at most 128 MiB of HBM per device.

```python
import math
import jax
import jax.numpy as jnp
from jax import lax

MODEL_WIDTH = 8192
QUERY_HEADS = 32
KEY_VALUE_HEADS = 8
HEAD_SIZE = 128
IMAGE_TOKENS = 1601
TEXT_TOKENS = 256
IMAGE_LOOKBACK = 4
MOST = 3
SPANS = 32
IMAGES = 32
TEXT = 8192
N_FSDP = 8


def gain_pair(key, stream_id):
    return jax.random.uniform(jax.random.fold_in(key, stream_id), (HEAD_SIZE,), jnp.float32, 0.5, 2.0)


def draw_query_gain(key, part):
    return gain_pair(key, 1)


def draw_key_gain(key, part):
    return gain_pair(key, 2)


def draw_admission(key, part):
    span_ids = jnp.arange(SPANS, dtype=jnp.int32)[:, None]
    image_ids = jnp.arange(IMAGES, dtype=jnp.int32)[None, :]
    distance = span_ids - image_ids
    candidate = (distance >= 1) & (distance <= IMAGE_LOOKBACK)
    priority = jax.random.randint(jax.random.fold_in(key, 1), (SPANS, IMAGES), 0, 1 << 20, dtype=jnp.int32) * IMAGES + image_ids
    outranked = jnp.sum((priority[:, None, :] > priority[:, :, None]) & candidate[:, None, :], axis=2)
    crowded = jax.random.randint(jax.random.fold_in(key, 2), (SPANS,), 0, 4, dtype=jnp.int32) == 0
    forced = jax.random.randint(jax.random.fold_in(key, 3), (), IMAGE_LOOKBACK, SPANS, dtype=jnp.int32)
    span_line = jnp.arange(SPANS, dtype=jnp.int32)
    crowded = crowded | (span_line == forced) | (span_line == SPANS - 1)
    extra_slots = jnp.where(crowded, MOST - 1, 0)[:, None]
    admitted = (distance == 0) | candidate & (outranked < extra_slots)
    return admitted.astype(jnp.int32)


def steps_of(rng, extent, split, least, high):
    factor_of = 1.0
    for position, blocks in split:
        draws = jax.random.uniform(jax.random.fold_in(jax.random.fold_in(rng, 6), position), (blocks,), jnp.float32, least / len(split), high / len(split))
        factor_of = factor_of * jnp.repeat(jnp.exp(draws), extent[position] // blocks).reshape((-1,) + (1,) * (len(extent) - 1 - position))
    return factor_of


def centred(own_key, shape, scale, limit, split=(), held_as=jnp.bfloat16):
    drawn = jax.random.normal(own_key, shape, jnp.float32) * scale
    if len(split) > 0:
        drawn = steps_of(own_key, shape, split, -0.22, 0.18) * drawn
    return jnp.clip(drawn, min=-limit, max=limit).astype(held_as)


def setup_inputs(seed: int = 0) -> dict:
    splits = jax.random.split(jax.random.key(seed), 9)
    return {
        "text_states": centred(splits[0], (TEXT, MODEL_WIDTH), 1.0, 6.0, ((0, 32),)),
        "images": centred(splits[1], (IMAGES, IMAGE_TOKENS, MODEL_WIDTH), 1.0, 6.0, ((0, 32), (2, 8))),
        "norm_gain": jnp.clip(1.0 + 0.18 * jax.random.normal(splits[2], (MODEL_WIDTH,), jnp.float32), 0.1, 1.9),
        "query_weight": centred(splits[3], (MODEL_WIDTH, QUERY_HEADS * HEAD_SIZE), MODEL_WIDTH ** -0.5, 0.0625, ((0, 32), (1, 8))),
        "image_projection_weight": centred(splits[4], (MODEL_WIDTH, KEY_VALUE_HEADS * 2 * HEAD_SIZE), MODEL_WIDTH ** -0.5, 0.0625, ((0, 256),)),
        "query_gain": draw_query_gain(jax.random.fold_in(splits[8], 71), 0),
        "key_gain": draw_key_gain(jax.random.fold_in(splits[8], 71), 0),
        "admission": draw_admission(jax.random.fold_in(splits[8], 71), 0),
    }


def rms_scale(values, gain):
    return values * lax.rsqrt(lax.optimization_barrier(jnp.mean(values * values, axis=-1, keepdims=True)) + 1e-05) * gain

def reference(text_states, images, norm_gain, query_weight, image_projection_weight, query_gain, key_gain, admission):
    normed = rms_scale(text_states.astype(jnp.float32), norm_gain).astype(jnp.bfloat16)
    queries = jnp.dot(normed, query_weight, preferred_element_type=jnp.float32).reshape(TEXT, QUERY_HEADS, HEAD_SIZE)
    query_heads = rms_scale(queries, query_gain).astype(jnp.bfloat16)
    block_width = MODEL_WIDTH // N_FSDP

    def project(image_rows):
        score_product = jnp.zeros((IMAGE_TOKENS, KEY_VALUE_HEADS * 2 * HEAD_SIZE), jnp.float32)
        for block in range(N_FSDP):
            partial_term = jnp.dot(image_rows[:, block * block_width:(block + 1) * block_width], image_projection_weight[block * block_width:(block + 1) * block_width], preferred_element_type=jnp.float32)
            rounded_term = lax.optimization_barrier(partial_term.astype(jnp.bfloat16))
            score_product = score_product + rounded_term.astype(jnp.float32)
        score_product = score_product.reshape(IMAGE_TOKENS, KEY_VALUE_HEADS, 2 * HEAD_SIZE)
        key_part = rms_scale(score_product[..., :HEAD_SIZE], key_gain)
        packed = jnp.concatenate([key_part, score_product[..., HEAD_SIZE:]], axis=-1).astype(jnp.bfloat16)
        return jnp.transpose(packed, (1, 0, 2))
    image_key_value = lax.map(project, images)
    padded_images = jnp.concatenate([jnp.zeros((IMAGE_LOOKBACK, KEY_VALUE_HEADS, IMAGE_TOKENS, 2 * HEAD_SIZE), jnp.bfloat16), image_key_value], axis=0)
    heads_per_group = QUERY_HEADS // KEY_VALUE_HEADS
    score_scale = 1.0 / math.sqrt(HEAD_SIZE)

    def span_out(operands):
        span_index, query_block_rows, admit_row = operands
        image_window = lax.dynamic_slice_in_dim(padded_images, span_index, IMAGE_LOOKBACK + 1, 0)
        image_ids = span_index - IMAGE_LOOKBACK + jnp.arange(IMAGE_LOOKBACK + 1, dtype=jnp.int32)
        admitted = (image_ids >= 0) & (jnp.take(admit_row, jnp.maximum(image_ids, 0).astype(jnp.int32)) == 1)
        column_live = jnp.repeat(admitted, IMAGE_TOKENS)
        key_value_pair = jnp.moveaxis(image_window, 1, 0).reshape(KEY_VALUE_HEADS, (IMAGE_LOOKBACK + 1) * IMAGE_TOKENS, 2 * HEAD_SIZE).astype(jnp.float32)
        query_widened = query_block_rows.reshape(TEXT_TOKENS, KEY_VALUE_HEADS, heads_per_group, HEAD_SIZE).astype(jnp.float32)
        scores = jnp.einsum('tkgd,knd->kgtn', query_widened, key_value_pair[..., :HEAD_SIZE]) * score_scale
        scores = jnp.where(column_live, scores, -jnp.inf)
        row_peak = lax.optimization_barrier(jnp.max(scores, axis=-1, keepdims=True))
        weights = jnp.exp(scores - row_peak)
        row_total = lax.optimization_barrier(jnp.sum(weights, axis=-1, keepdims=True))
        rounded = lax.optimization_barrier(weights.astype(jnp.bfloat16)).astype(jnp.float32)
        blended = jnp.einsum('kgtn,knd->tkgd', rounded, key_value_pair[..., HEAD_SIZE:])
        blended = blended / jnp.transpose(row_total, (2, 0, 1, 3))
        return blended.reshape(TEXT_TOKENS, QUERY_HEADS * HEAD_SIZE).astype(jnp.bfloat16)
    span_outputs = lax.map(span_out, (jnp.arange(SPANS, dtype=jnp.int32), query_heads.reshape(SPANS, TEXT_TOKENS, QUERY_HEADS, HEAD_SIZE), admission))
    return span_outputs.reshape(TEXT, QUERY_HEADS * HEAD_SIZE)
```

```python
import math

import jax
import jax.numpy as jnp
from jax import lax
from jax.sharding import PartitionSpec as P

KEY_VALUE_HEADS = 8
IMAGE_LOOKBACK = 4


def from_behind(value, axis, steps):
    count = lax.axis_size(axis)
    initial, last = (max(0, -steps), min(count, count - steps))
    return lax.ppermute(value, axis, [(source, source + steps) for source in range(initial, last)])


def rms_scale(values, gain):
    return values * lax.rsqrt(jnp.mean(values * values, axis=-1, keepdims=True) + 1e-05) * gain


def attend(query_heads, stacked, admitted):
    slot_count, kv_heads, image_tokens, double_width = stacked.shape
    head_dim = double_width // 2
    row_count, heads_local, _ = query_heads.shape
    heads_per_group = heads_local // kv_heads
    grouped = query_heads.reshape(row_count, kv_heads, heads_per_group, head_dim)
    grouped = grouped.transpose(1, 2, 0, 3).reshape(kv_heads, heads_per_group * row_count, head_dim)
    per_head = jnp.moveaxis(stacked, 1, 0).reshape(
        kv_heads, slot_count * image_tokens, double_width
    )
    column_live = jnp.repeat(admitted, image_tokens)
    score_scale = 1.0 / math.sqrt(head_dim)

    def one_head(operands):
        query_rows, key_value_pair = operands
        scores = (
            lax.dot_general(
                query_rows,
                key_value_pair[:, :head_dim],
                (((1,), (1,)), ((), ())),
                preferred_element_type=jnp.float32,
            )
            * score_scale
        )
        scores = jnp.where(column_live[None, :], scores, -jnp.inf)
        row_peak = jnp.max(scores, axis=1, keepdims=True)
        weights = jnp.exp(scores - row_peak)
        row_total = jnp.sum(weights, axis=1, keepdims=True)
        blended = jnp.dot(
            weights.astype(jnp.bfloat16),
            key_value_pair[:, head_dim:],
            preferred_element_type=jnp.float32,
        )
        return blended / row_total

    outputs = lax.map(one_head, (grouped, per_head))
    outputs = outputs.reshape(kv_heads, heads_per_group, row_count, head_dim).transpose(2, 0, 1, 3)
    return outputs.reshape(row_count, heads_local * head_dim).astype(jnp.bfloat16)


def on_device(
    text_states,
    images,
    norm_gain,
    query_weight,
    image_projection_weight,
    query_gain,
    key_gain,
    admission,
):
    head_dim = query_gain.shape[0]
    local_key_value = KEY_VALUE_HEADS // lax.axis_size("fsdp")
    heads_local = query_weight.shape[1] // head_dim
    row_count = text_states.shape[0]
    normed = rms_scale(text_states.astype(jnp.float32), norm_gain).astype(jnp.bfloat16)
    kv_rows, kv_width = image_projection_weight.shape
    query_width = query_weight.shape[1]
    kv_as_rows = image_projection_weight.reshape(kv_rows * kv_width // query_width, query_width)
    both = lax.all_gather(
        jnp.concatenate([kv_as_rows, query_weight], axis=0), "seq", axis=0, tiled=False
    )
    weight_block = both[:, : kv_as_rows.shape[0]].reshape(-1, kv_width)
    query_block = both[:, kv_as_rows.shape[0] :].reshape(-1, query_width)
    queries = jnp.dot(normed, query_block, preferred_element_type=jnp.float32)
    query_heads = rms_scale(queries.reshape(row_count, heads_local, head_dim), query_gain).astype(
        jnp.bfloat16
    )
    features = images[0]
    columns = weight_block
    score_product = jnp.dot(features, columns, preferred_element_type=jnp.float32)
    own_kv = lax.psum_scatter(
        score_product.reshape(
            features.shape[0], local_key_value * lax.axis_size("fsdp"), 2 * head_dim
        )
        .transpose(1, 0, 2)
        .astype(jnp.bfloat16),
        "fsdp",
        scatter_dimension=0,
        tiled=True,
    ).astype(jnp.float32)
    key_part = rms_scale(own_kv[..., :head_dim], key_gain)
    packed = jnp.concatenate([key_part, own_kv[..., head_dim:]], axis=-1).astype(jnp.bfloat16)
    image_window = [packed]
    for distance in range(1, IMAGE_LOOKBACK + 1):
        image_window.append(from_behind(packed, "seq", distance))
    stacked = jnp.stack(image_window)
    span_index = lax.axis_index("seq")
    image_ids = span_index - jnp.arange(IMAGE_LOOKBACK + 1, dtype=jnp.int32)
    admitted = (image_ids >= 0) & (jnp.take(admission[0], jnp.maximum(image_ids, 0)) == 1)
    return attend(query_heads, stacked, admitted)


def solution(mesh):
    placed = (
        P("seq", None),
        P("seq", None, "fsdp"),
        P(),
        P("seq", "fsdp"),
        P(("fsdp", "seq"), None),
        P(),
        P(),
        P("seq", None),
    )
    return jax.shard_map(
        on_device, mesh=mesh, in_specs=placed, out_specs=P("seq", "fsdp"), check_vma=False
    )
```

```python
import math

import jax
import jax.numpy as jnp
from jax import lax
from jax.sharding import PartitionSpec as P

KEY_VALUE_HEADS = 8
IMAGE_LOOKBACK = 4


def from_behind(value, axis, steps):
    count = lax.axis_size(axis)
    initial, last = (max(0, -steps), min(count, count - steps))
    return lax.ppermute(value, axis, [(source, source + steps) for source in range(initial, last)])


def rms_scale(values, gain):
    return values * lax.rsqrt(jnp.mean(values * values, axis=-1, keepdims=True) + 1e-05) * gain


def attend(query_heads, stacked, admitted):
    slot_count, kv_heads, image_tokens, double_width = stacked.shape
    head_dim = double_width // 2
    row_count, heads_local, _ = query_heads.shape
    heads_per_group = heads_local // kv_heads
    grouped = query_heads.reshape(row_count, kv_heads, heads_per_group, head_dim)
    grouped = grouped.transpose(1, 2, 0, 3).reshape(kv_heads, heads_per_group * row_count, head_dim)
    per_head = jnp.moveaxis(stacked, 1, 0).reshape(
        kv_heads, slot_count * image_tokens, double_width
    )
    column_live = jnp.repeat(admitted, image_tokens)
    score_scale = 1.0 / math.sqrt(head_dim)

    def one_head(operands):
        query_rows, key_value_pair = operands
        scores = (
            lax.dot_general(
                query_rows,
                key_value_pair[:, :head_dim],
                (((1,), (1,)), ((), ())),
                preferred_element_type=jnp.float32,
            )
            * score_scale
        )
        scores = jnp.where(column_live[None, :], scores, -jnp.inf)
        row_peak = jnp.max(scores, axis=1, keepdims=True)
        weights = jnp.exp(scores - row_peak)
        row_total = jnp.sum(weights, axis=1, keepdims=True)
        blended = jnp.dot(
            weights.astype(jnp.bfloat16),
            key_value_pair[:, head_dim:],
            preferred_element_type=jnp.float32,
        )
        return blended / row_total

    outputs = lax.map(one_head, (grouped, per_head))
    outputs = outputs.reshape(kv_heads, heads_per_group, row_count, head_dim).transpose(2, 0, 1, 3)
    return outputs.reshape(row_count, heads_local * head_dim).astype(jnp.bfloat16)


def on_device(
    text_states,
    images,
    norm_gain,
    query_weight,
    image_projection_weight,
    query_gain,
    key_gain,
    admission,
):
    head_dim = query_gain.shape[0]
    local_key_value = KEY_VALUE_HEADS // lax.axis_size("fsdp")
    heads_local = query_weight.shape[1] // head_dim
    row_count = text_states.shape[0]
    normed = rms_scale(text_states.astype(jnp.float32), norm_gain).astype(jnp.bfloat16)
    kv_rows, kv_width = image_projection_weight.shape
    query_width = query_weight.shape[1]
    column_blocks = kv_width // query_width
    kv_as_rows = (
        image_projection_weight.reshape(kv_rows, column_blocks, query_width)
        .transpose(1, 0, 2)
        .reshape(column_blocks * kv_rows, query_width)
    )
    both = lax.all_gather(
        jnp.concatenate([kv_as_rows, query_weight], axis=0), "seq", axis=0, tiled=False
    )
    query_block = both[:, column_blocks * kv_rows :].reshape(-1, query_width)
    queries = jnp.dot(normed, query_block, preferred_element_type=jnp.float32)
    query_heads = rms_scale(queries.reshape(row_count, heads_local, head_dim), query_gain).astype(
        jnp.bfloat16
    )
    features = images[0]
    score_product = jnp.concatenate(
        [
            jnp.dot(
                features,
                both[:, block * kv_rows : (block + 1) * kv_rows].reshape(-1, query_width),
                preferred_element_type=jnp.float32,
            )
            for block in range(column_blocks)
        ],
        axis=1,
    )
    own_kv = lax.psum_scatter(
        score_product.reshape(
            features.shape[0], local_key_value * lax.axis_size("fsdp"), 2 * head_dim
        )
        .transpose(1, 0, 2)
        .astype(jnp.bfloat16),
        "fsdp",
        scatter_dimension=0,
        tiled=True,
    ).astype(jnp.float32)
    key_part = rms_scale(own_kv[..., :head_dim], key_gain)
    packed = jnp.concatenate([key_part, own_kv[..., head_dim:]], axis=-1).astype(jnp.bfloat16)
    image_window = [packed]
    for distance in range(1, IMAGE_LOOKBACK + 1):
        image_window.append(from_behind(packed, "seq", distance))
    stacked = jnp.stack(image_window)
    span_index = lax.axis_index("seq")
    image_ids = span_index - jnp.arange(IMAGE_LOOKBACK + 1, dtype=jnp.int32)
    admitted = (image_ids >= 0) & (jnp.take(admission[0], jnp.maximum(image_ids, 0)) == 1)
    return attend(query_heads, stacked, admitted)


def solution(mesh):
    placed = (
        P("seq", None),
        P("seq", None, "fsdp"),
        P(),
        P("seq", "fsdp"),
        P(("fsdp", "seq"), None),
        P(),
        P(),
        P("seq", None),
    )
    return jax.shard_map(
        on_device, mesh=mesh, in_specs=placed, out_specs=P("seq", "fsdp"), check_vma=False
    )
```

```python
import math

import jax
import jax.numpy as jnp
from jax import lax
from jax.sharding import PartitionSpec as P

KEY_VALUE_HEADS = 8
IMAGE_LOOKBACK = 4


def from_behind(value, axis, steps):
    count = lax.axis_size(axis)
    initial, last = (max(0, -steps), min(count, count - steps))
    return lax.ppermute(value, axis, [(source, source + steps) for source in range(initial, last)])


def rms_scale(values, gain):
    return values * lax.rsqrt(jnp.mean(values * values, axis=-1, keepdims=True) + 1e-05) * gain


def attend_part(grouped, key_value_pair, column_live):
    head_dim = grouped.shape[-1]
    scores = jnp.einsum(
        "kqd,knd->kqn", grouped, key_value_pair[..., :head_dim], preferred_element_type=jnp.float32
    ) * (1.0 / math.sqrt(head_dim))
    scores = jnp.where(column_live[None, None, :], scores, -jnp.inf)
    row_peak = jnp.max(scores, axis=-1, keepdims=True)
    weights = jnp.exp(scores - jnp.where(row_peak == -jnp.inf, 0.0, row_peak))
    row_total = jnp.sum(weights, axis=-1, keepdims=True)
    blended = jnp.einsum(
        "kqn,knd->kqd",
        weights.astype(jnp.bfloat16),
        key_value_pair[..., head_dim:],
        preferred_element_type=jnp.float32,
    )
    return row_peak, row_total, blended


def attend(query_heads, own, own_live, earlier, earlier_live):
    kv_heads, _, double_width = own.shape
    head_dim = double_width // 2
    row_count, heads_local, _ = query_heads.shape
    heads_per_group = heads_local // kv_heads
    grouped = query_heads.reshape(row_count, kv_heads, heads_per_group, head_dim)
    grouped = grouped.transpose(1, 2, 0, 3).reshape(kv_heads, heads_per_group * row_count, head_dim)
    own_peak, own_total, own_blend = attend_part(grouped, own, own_live)
    far_peak, far_total, far_blend = attend_part(grouped, earlier, earlier_live)
    peak = jnp.maximum(own_peak, far_peak)
    own_scale = jnp.exp(own_peak - peak)
    far_scale = jnp.exp(far_peak - peak)
    outputs = (own_blend * own_scale + far_blend * far_scale) / (
        own_total * own_scale + far_total * far_scale
    )
    outputs = outputs.reshape(kv_heads, heads_per_group, row_count, head_dim).transpose(2, 0, 1, 3)
    return outputs.reshape(row_count, heads_local * head_dim).astype(jnp.bfloat16)


def on_device(
    text_states,
    images,
    norm_gain,
    query_weight,
    image_projection_weight,
    query_gain,
    key_gain,
    admission,
):
    head_dim = query_gain.shape[0]
    local_key_value = KEY_VALUE_HEADS // lax.axis_size("fsdp")
    heads_local = query_weight.shape[1] // head_dim
    row_count = text_states.shape[0]
    normed = rms_scale(text_states.astype(jnp.float32), norm_gain).astype(jnp.bfloat16)
    kv_rows, kv_width = image_projection_weight.shape
    query_width = query_weight.shape[1]
    column_blocks = kv_width // query_width
    kv_as_rows = (
        image_projection_weight.reshape(kv_rows, column_blocks, query_width)
        .transpose(1, 0, 2)
        .reshape(column_blocks * kv_rows, query_width)
    )
    both = lax.all_gather(
        jnp.concatenate([kv_as_rows, query_weight], axis=0), "seq", axis=0, tiled=False
    )
    query_block = both[:, column_blocks * kv_rows :].reshape(-1, query_width)
    queries = jnp.dot(normed, query_block, preferred_element_type=jnp.float32)
    query_heads = rms_scale(queries.reshape(row_count, heads_local, head_dim), query_gain).astype(
        jnp.bfloat16
    )
    features = images[0]
    score_product = jnp.concatenate(
        [
            jnp.dot(
                features,
                both[:, block * kv_rows : (block + 1) * kv_rows].reshape(-1, query_width),
                preferred_element_type=jnp.float32,
            )
            for block in range(column_blocks)
        ],
        axis=1,
    )
    own_kv = lax.psum_scatter(
        score_product.reshape(
            features.shape[0], local_key_value * lax.axis_size("fsdp"), 2 * head_dim
        )
        .transpose(1, 0, 2)
        .astype(jnp.bfloat16),
        "fsdp",
        scatter_dimension=0,
        tiled=True,
    ).astype(jnp.float32)
    key_part = rms_scale(own_kv[..., :head_dim], key_gain)
    packed = jnp.concatenate([key_part, own_kv[..., head_dim:]], axis=-1).astype(jnp.bfloat16)
    span_index = lax.axis_index("seq")
    image_ids = span_index - jnp.arange(IMAGE_LOOKBACK + 1, dtype=jnp.int32)
    admitted = (image_ids >= 0) & (jnp.take(admission[0], jnp.maximum(image_ids, 0)) == 1)
    earlier_admitted = admitted[1:]
    nearest = jnp.argmax(earlier_admitted)
    farthest = IMAGE_LOOKBACK - 1 - jnp.argmax(earlier_admitted[::-1])
    admitted_count = jnp.sum(earlier_admitted.astype(jnp.int32))
    received = [from_behind(packed, "seq", distance) for distance in range(1, IMAGE_LOOKBACK + 1)]

    def pick(slot):
        chosen = received[-1]
        for distance in range(IMAGE_LOOKBACK - 2, -1, -1):
            chosen = jnp.where(slot == distance, received[distance], chosen)
        return chosen

    earlier = jnp.concatenate([pick(nearest), pick(farthest)], axis=1)
    image_tokens = packed.shape[1]
    earlier_live = jnp.concatenate(
        [
            jnp.broadcast_to(admitted_count >= 1, (image_tokens,)),
            jnp.broadcast_to(admitted_count >= 2, (image_tokens,)),
        ]
    )
    own_live = jnp.broadcast_to(admitted[0], (image_tokens,))
    return attend(query_heads, packed, own_live, earlier, earlier_live)


def solution(mesh):
    placed = (
        P("seq", None),
        P("seq", None, "fsdp"),
        P(),
        P("seq", "fsdp"),
        P(("fsdp", "seq"), None),
        P(),
        P(),
        P("seq", None),
    )
    return jax.shard_map(
        on_device, mesh=mesh, in_specs=placed, out_specs=P("seq", "fsdp"), check_vma=False
    )
```

```python
import math

import jax
import jax.numpy as jnp
from jax import lax
from jax.sharding import PartitionSpec as P

KEY_VALUE_HEADS = 8
IMAGE_LOOKBACK = 4


def from_behind(value, axis, steps):
    count = lax.axis_size(axis)
    initial, last = (max(0, -steps), min(count, count - steps))
    return lax.ppermute(value, axis, [(source, source + steps) for source in range(initial, last)])


def rms_scale(values, gain):
    return values * lax.rsqrt(jnp.mean(values * values, axis=-1, keepdims=True) + 1e-05) * gain


def attend_part(grouped, key_value_pair, column_live):
    head_dim = grouped.shape[-1]
    scores = jnp.einsum(
        "kqd,knd->kqn", grouped, key_value_pair[..., :head_dim], preferred_element_type=jnp.float32
    ) * (1.0 / math.sqrt(head_dim))
    scores = jnp.where(column_live[None, None, :], scores, -jnp.inf)
    row_peak = jnp.max(scores, axis=-1, keepdims=True)
    weights = jnp.exp(scores - jnp.where(row_peak == -jnp.inf, 0.0, row_peak))
    row_total = jnp.sum(weights, axis=-1, keepdims=True)
    blended = jnp.einsum(
        "kqn,knd->kqd",
        weights.astype(jnp.bfloat16),
        key_value_pair[..., head_dim:],
        preferred_element_type=jnp.float32,
    )
    return row_peak, row_total, blended


def attend(query_heads, own, own_live, earlier, earlier_live):
    kv_heads, _, double_width = own.shape
    head_dim = double_width // 2
    row_count, heads_local, _ = query_heads.shape
    heads_per_group = heads_local // kv_heads
    grouped = query_heads.reshape(row_count, kv_heads, heads_per_group, head_dim)
    grouped = grouped.transpose(1, 2, 0, 3).reshape(kv_heads, heads_per_group * row_count, head_dim)
    own_peak, own_total, own_blend = attend_part(grouped, own, own_live)
    far_peak, far_total, far_blend = attend_part(grouped, earlier, earlier_live)
    peak = jnp.maximum(own_peak, far_peak)
    own_scale = jnp.exp(own_peak - peak)
    far_scale = jnp.exp(far_peak - peak)
    outputs = (own_blend * own_scale + far_blend * far_scale) / (
        own_total * own_scale + far_total * far_scale
    )
    outputs = outputs.reshape(kv_heads, heads_per_group, row_count, head_dim).transpose(2, 0, 1, 3)
    return outputs.reshape(row_count, heads_local * head_dim).astype(jnp.bfloat16)


def on_device(
    text_states,
    images,
    norm_gain,
    query_weight,
    image_projection_weight,
    query_gain,
    key_gain,
    admission,
):
    head_dim = query_gain.shape[0]
    local_key_value = KEY_VALUE_HEADS // lax.axis_size("fsdp")
    heads_local = query_weight.shape[1] // head_dim
    row_count = text_states.shape[0]
    normed = rms_scale(text_states.astype(jnp.float32), norm_gain).astype(jnp.bfloat16)
    weight_block = lax.all_gather(image_projection_weight, "seq", axis=0, tiled=True)
    query_block = lax.all_gather(query_weight, "seq", axis=0, tiled=True)
    features = images[0]
    pair_width = 2 * head_dim
    head_count = weight_block.shape[1] // pair_width
    partials = jnp.stack(
        [
            jnp.dot(
                features,
                weight_block[:, head * pair_width : (head + 1) * pair_width],
                preferred_element_type=jnp.float32,
            ).astype(jnp.bfloat16)
            for head in range(head_count)
        ]
    )
    gathered_partials = lax.all_to_all(partials, "fsdp", 0, 0, tiled=True)
    own_kv = jnp.sum(gathered_partials.astype(jnp.float32), axis=0, keepdims=True)
    queries = jnp.dot(normed, query_block, preferred_element_type=jnp.float32)
    query_heads = rms_scale(queries.reshape(row_count, heads_local, head_dim), query_gain).astype(
        jnp.bfloat16
    )
    key_part = rms_scale(own_kv[..., :head_dim], key_gain)
    packed = jnp.concatenate([key_part, own_kv[..., head_dim:]], axis=-1).astype(jnp.bfloat16)
    span_index = lax.axis_index("seq")
    image_ids = span_index - jnp.arange(IMAGE_LOOKBACK + 1, dtype=jnp.int32)
    admitted = (image_ids >= 0) & (jnp.take(admission[0], jnp.maximum(image_ids, 0)) == 1)
    earlier_admitted = admitted[1:]
    nearest = jnp.argmax(earlier_admitted)
    farthest = IMAGE_LOOKBACK - 1 - jnp.argmax(earlier_admitted[::-1])
    admitted_count = jnp.sum(earlier_admitted.astype(jnp.int32))
    received = [from_behind(packed, "seq", distance) for distance in range(1, IMAGE_LOOKBACK + 1)]

    def pick(slot):
        chosen = received[-1]
        for distance in range(IMAGE_LOOKBACK - 2, -1, -1):
            chosen = jnp.where(slot == distance, received[distance], chosen)
        return chosen

    earlier = jnp.concatenate([pick(nearest), pick(farthest)], axis=1)
    image_tokens = packed.shape[1]
    earlier_live = jnp.concatenate(
        [
            jnp.broadcast_to(admitted_count >= 1, (image_tokens,)),
            jnp.broadcast_to(admitted_count >= 2, (image_tokens,)),
        ]
    )
    own_live = jnp.broadcast_to(admitted[0], (image_tokens,))
    return attend(query_heads, packed, own_live, earlier, earlier_live)


def solution(mesh):
    placed = (
        P("seq", None),
        P("seq", None, "fsdp"),
        P(),
        P("seq", "fsdp"),
        P(("fsdp", "seq"), None),
        P(),
        P(),
        P("seq", None),
    )
    return jax.shard_map(
        on_device, mesh=mesh, in_specs=placed, out_specs=P("seq", "fsdp"), check_vma=False
    )
```

```python
import math

import jax
import jax.numpy as jnp
from jax import lax
from jax.sharding import PartitionSpec as P

KEY_VALUE_HEADS = 8
IMAGE_LOOKBACK = 4


def from_behind(value, axis, steps):
    count = lax.axis_size(axis)
    initial, last = (max(0, -steps), min(count, count - steps))
    return lax.ppermute(value, axis, [(source, source + steps) for source in range(initial, last)])


def rms_scale(values, gain):
    return values * lax.rsqrt(jnp.mean(values * values, axis=-1, keepdims=True) + 1e-05) * gain


def attend_part(grouped, key_value_pair, column_live):
    head_dim = grouped.shape[-1]
    scores = jnp.einsum(
        "kqd,knd->kqn", grouped, key_value_pair[..., :head_dim], preferred_element_type=jnp.float32
    ) * (1.0 / math.sqrt(head_dim))
    scores = jnp.where(column_live[None, None, :], scores, -jnp.inf)
    row_peak = jnp.max(scores, axis=-1, keepdims=True)
    weights = jnp.exp(scores - jnp.where(row_peak == -jnp.inf, 0.0, row_peak))
    row_total = jnp.sum(weights, axis=-1, keepdims=True)
    blended = jnp.einsum(
        "kqn,knd->kqd",
        weights.astype(jnp.bfloat16),
        key_value_pair[..., head_dim:],
        preferred_element_type=jnp.float32,
    )
    return row_peak, row_total, blended


def attend(query_heads, own, own_live, earlier, earlier_live):
    kv_heads, _, double_width = own.shape
    head_dim = double_width // 2
    row_count, heads_local, _ = query_heads.shape
    heads_per_group = heads_local // kv_heads
    grouped = query_heads.reshape(row_count, kv_heads, heads_per_group, head_dim)
    grouped = grouped.transpose(1, 2, 0, 3).reshape(kv_heads, heads_per_group * row_count, head_dim)
    own_peak, own_total, own_blend = attend_part(grouped, own, own_live)
    far_peak, far_total, far_blend = attend_part(grouped, earlier, earlier_live)
    peak = jnp.maximum(own_peak, far_peak)
    own_scale = jnp.exp(own_peak - peak)
    far_scale = jnp.exp(far_peak - peak)
    outputs = (own_blend * own_scale + far_blend * far_scale) / (
        own_total * own_scale + far_total * far_scale
    )
    outputs = outputs.reshape(kv_heads, heads_per_group, row_count, head_dim).transpose(2, 0, 1, 3)
    return outputs.reshape(row_count, heads_local * head_dim).astype(jnp.bfloat16)


def on_device(
    text_states,
    images,
    norm_gain,
    query_weight,
    image_projection_weight,
    query_gain,
    key_gain,
    admission,
):
    head_dim = query_gain.shape[0]
    local_key_value = KEY_VALUE_HEADS // lax.axis_size("fsdp")
    heads_local = query_weight.shape[1] // head_dim
    row_count = text_states.shape[0]
    normed = rms_scale(text_states.astype(jnp.float32), norm_gain).astype(jnp.bfloat16)
    kv_rows, kv_width = image_projection_weight.shape
    query_width = query_weight.shape[1]
    column_blocks = kv_width // query_width
    kv_as_rows = (
        image_projection_weight.reshape(kv_rows, column_blocks, query_width)
        .transpose(1, 0, 2)
        .reshape(column_blocks * kv_rows, query_width)
    )
    both = lax.all_gather(
        jnp.concatenate([kv_as_rows, query_weight], axis=0), "seq", axis=0, tiled=False
    )
    query_block = both[:, column_blocks * kv_rows :].reshape(-1, query_width)
    queries = jnp.dot(normed, query_block, preferred_element_type=jnp.float32)
    query_heads = rms_scale(queries.reshape(row_count, heads_local, head_dim), query_gain).astype(
        jnp.bfloat16
    )
    features = images[0]
    pair_width = 2 * head_dim
    pairs_per_block = query_width // pair_width
    partials = jnp.stack(
        [
            jnp.dot(
                features,
                both[:, block * kv_rows : (block + 1) * kv_rows, pair * pair_width : (pair + 1) * pair_width]
                .reshape(-1, pair_width),
                preferred_element_type=jnp.float32,
            ).astype(jnp.bfloat16)
            for block in range(column_blocks)
            for pair in range(pairs_per_block)
        ]
    )
    own_kv = lax.psum_scatter(partials, "fsdp", scatter_dimension=0, tiled=True).astype(jnp.float32)
    key_part = rms_scale(own_kv[..., :head_dim], key_gain)
    packed = jnp.concatenate([key_part, own_kv[..., head_dim:]], axis=-1).astype(jnp.bfloat16)
    span_index = lax.axis_index("seq")
    image_ids = span_index - jnp.arange(IMAGE_LOOKBACK + 1, dtype=jnp.int32)
    admitted = (image_ids >= 0) & (jnp.take(admission[0], jnp.maximum(image_ids, 0)) == 1)
    earlier_admitted = admitted[1:]
    nearest = jnp.argmax(earlier_admitted)
    farthest = IMAGE_LOOKBACK - 1 - jnp.argmax(earlier_admitted[::-1])
    admitted_count = jnp.sum(earlier_admitted.astype(jnp.int32))
    two_behind = from_behind(packed, "seq", 2)
    four_behind = from_behind(packed, "seq", 4)
    partner = lax.ppermute(
        jnp.stack([packed, two_behind, four_behind]),
        "seq",
        [(source, source ^ 1) for source in range(lax.axis_size("seq"))],
    )
    first_core = span_index % 2 == 0
    received = [
        jnp.where(first_core, partner[1], partner[0]),
        two_behind,
        jnp.where(first_core, partner[2], partner[1]),
        four_behind,
    ]

    def pick(slot):
        chosen = received[-1]
        for distance in range(IMAGE_LOOKBACK - 2, -1, -1):
            chosen = jnp.where(slot == distance, received[distance], chosen)
        return chosen

    earlier = jnp.concatenate([pick(nearest), pick(farthest)], axis=1)
    image_tokens = packed.shape[1]
    earlier_live = jnp.concatenate(
        [
            jnp.broadcast_to(admitted_count >= 1, (image_tokens,)),
            jnp.broadcast_to(admitted_count >= 2, (image_tokens,)),
        ]
    )
    own_live = jnp.broadcast_to(admitted[0], (image_tokens,))
    return attend(query_heads, packed, own_live, earlier, earlier_live)


def solution(mesh):
    placed = (
        P("seq", None),
        P("seq", None, "fsdp"),
        P(),
        P("seq", "fsdp"),
        P(("fsdp", "seq"), None),
        P(),
        P(),
        P("seq", None),
    )
    return jax.shard_map(
        on_device, mesh=mesh, in_specs=placed, out_specs=P("seq", "fsdp"), check_vma=False
    )
```

```python
import math

import jax
import jax.numpy as jnp
from jax import lax
from jax.sharding import Mesh, PartitionSpec as P

KEY_VALUE_HEADS = 8
SEQ = ("chip", "core")
IMAGE_LOOKBACK = 4


def from_behind(value, axis, steps):
    count = lax.axis_size(axis)
    initial, last = (max(0, -steps), min(count, count - steps))
    return lax.ppermute(value, axis, [(source, source + steps) for source in range(initial, last)])


def rms_scale(values, gain):
    return values * lax.rsqrt(jnp.mean(values * values, axis=-1, keepdims=True) + 1e-05) * gain


def attend_part(grouped, key_value_pair, column_live):
    head_dim = grouped.shape[-1]
    scores = jnp.einsum(
        "kqd,knd->kqn", grouped, key_value_pair[..., :head_dim], preferred_element_type=jnp.float32
    ) * (1.0 / math.sqrt(head_dim))
    scores = jnp.where(column_live[None, None, :], scores, -jnp.inf)
    row_peak = jnp.max(scores, axis=-1, keepdims=True)
    weights = jnp.exp(scores - jnp.where(row_peak == -jnp.inf, 0.0, row_peak))
    row_total = jnp.sum(weights, axis=-1, keepdims=True)
    blended = jnp.einsum(
        "kqn,knd->kqd",
        weights.astype(jnp.bfloat16),
        key_value_pair[..., head_dim:],
        preferred_element_type=jnp.float32,
    )
    return row_peak, row_total, blended


def attend(query_heads, own, own_live, earlier, earlier_live):
    kv_heads, _, double_width = own.shape
    head_dim = double_width // 2
    row_count, heads_local, _ = query_heads.shape
    heads_per_group = heads_local // kv_heads
    grouped = query_heads.reshape(row_count, kv_heads, heads_per_group, head_dim)
    grouped = grouped.transpose(1, 2, 0, 3).reshape(kv_heads, heads_per_group * row_count, head_dim)
    own_peak, own_total, own_blend = attend_part(grouped, own, own_live)
    far_peak, far_total, far_blend = attend_part(grouped, earlier, earlier_live)
    peak = jnp.maximum(own_peak, far_peak)
    own_scale = jnp.exp(own_peak - peak)
    far_scale = jnp.exp(far_peak - peak)
    outputs = (own_blend * own_scale + far_blend * far_scale) / (
        own_total * own_scale + far_total * far_scale
    )
    outputs = outputs.reshape(kv_heads, heads_per_group, row_count, head_dim).transpose(2, 0, 1, 3)
    return outputs.reshape(row_count, heads_local * head_dim).astype(jnp.bfloat16)


def on_device(
    text_states,
    images,
    norm_gain,
    query_weight,
    image_projection_weight,
    query_gain,
    key_gain,
    admission,
):
    head_dim = query_gain.shape[0]
    local_key_value = KEY_VALUE_HEADS // lax.axis_size("fsdp")
    heads_local = query_weight.shape[1] // head_dim
    row_count = text_states.shape[0]
    normed = rms_scale(text_states.astype(jnp.float32), norm_gain).astype(jnp.bfloat16)
    kv_rows, kv_width = image_projection_weight.shape
    query_width = query_weight.shape[1]
    column_blocks = kv_width // query_width
    kv_as_rows = (
        image_projection_weight.reshape(kv_rows, column_blocks, query_width)
        .transpose(1, 0, 2)
        .reshape(column_blocks * kv_rows, query_width)
    )
    stacked_rows = jnp.concatenate([kv_as_rows, query_weight], axis=0)
    mine = lax.all_gather(stacked_rows, "chip", axis=0, tiled=False)
    swap = [(0, 1), (1, 0)]
    other_kv = lax.ppermute(mine[:, : column_blocks * kv_rows], "core", swap)
    other_query = lax.ppermute(mine[:, column_blocks * kv_rows :], "core", swap)
    first_core = lax.axis_index("core") == 0
    chip_count = mine.shape[0]

    def by_parity(columns, block):
        split = columns.reshape(columns.shape[0], chip_count, 2, block)
        even = split[:, :, 0].reshape(columns.shape[0], chip_count * block)
        odd = split[:, :, 1].reshape(columns.shape[0], chip_count * block)
        return jnp.where(first_core, even, odd), jnp.where(first_core, odd, even)

    normed_mine, normed_other = by_parity(normed, query_weight.shape[0])
    query_mine = mine[:, column_blocks * kv_rows :].reshape(-1, query_width)
    queries = jnp.dot(normed_mine, query_mine, preferred_element_type=jnp.float32) + jnp.dot(
        normed_other, other_query.reshape(-1, query_width), preferred_element_type=jnp.float32
    )
    query_heads = rms_scale(queries.reshape(row_count, heads_local, head_dim), query_gain).astype(
        jnp.bfloat16
    )
    features_mine, features_other = by_parity(images[0], kv_rows)
    pair_width = 2 * head_dim
    pairs_per_block = query_width // pair_width

    def head_weight(rows, block, pair):
        return rows[:, block * kv_rows : (block + 1) * kv_rows, pair * pair_width : (pair + 1) * pair_width].reshape(
            -1, pair_width
        )

    partials = jnp.stack(
        [
            (
                jnp.dot(features_mine, head_weight(mine, block, pair), preferred_element_type=jnp.float32)
                + jnp.dot(features_other, head_weight(other_kv, block, pair), preferred_element_type=jnp.float32)
            ).astype(jnp.bfloat16)
            for block in range(column_blocks)
            for pair in range(pairs_per_block)
        ]
    )
    own_kv = lax.psum_scatter(partials, "fsdp", scatter_dimension=0, tiled=True).astype(jnp.float32)
    key_part = rms_scale(own_kv[..., :head_dim], key_gain)
    packed = jnp.concatenate([key_part, own_kv[..., head_dim:]], axis=-1).astype(jnp.bfloat16)
    span_index = lax.axis_index(SEQ)
    image_ids = span_index - jnp.arange(IMAGE_LOOKBACK + 1, dtype=jnp.int32)
    admitted = (image_ids >= 0) & (jnp.take(admission[0], jnp.maximum(image_ids, 0)) == 1)
    earlier_admitted = admitted[1:]
    nearest = jnp.argmax(earlier_admitted)
    farthest = IMAGE_LOOKBACK - 1 - jnp.argmax(earlier_admitted[::-1])
    admitted_count = jnp.sum(earlier_admitted.astype(jnp.int32))
    two_behind = from_behind(packed, SEQ, 2)
    four_behind = from_behind(packed, SEQ, 4)
    partner = lax.ppermute(
        jnp.stack([packed, two_behind, four_behind]),
        SEQ,
        [(source, source ^ 1) for source in range(lax.axis_size(SEQ))],
    )
    first_core = span_index % 2 == 0
    received = [
        jnp.where(first_core, partner[1], partner[0]),
        two_behind,
        jnp.where(first_core, partner[2], partner[1]),
        four_behind,
    ]

    def pick(slot):
        chosen = received[-1]
        for distance in range(IMAGE_LOOKBACK - 2, -1, -1):
            chosen = jnp.where(slot == distance, received[distance], chosen)
        return chosen

    earlier = jnp.concatenate([pick(nearest), pick(farthest)], axis=1)
    image_tokens = packed.shape[1]
    earlier_live = jnp.concatenate(
        [
            jnp.broadcast_to(admitted_count >= 1, (image_tokens,)),
            jnp.broadcast_to(admitted_count >= 2, (image_tokens,)),
        ]
    )
    own_live = jnp.broadcast_to(admitted[0], (image_tokens,))
    return attend(query_heads, packed, own_live, earlier, earlier_live)


def solution(mesh):
    placed = (
        P(SEQ, None),
        P(SEQ, None, "fsdp"),
        P(),
        P(SEQ, "fsdp"),
        P(("fsdp",) + SEQ, None),
        P(),
        P(),
        P(SEQ, None),
    )
    rows, columns = mesh.devices.shape
    split_mesh = Mesh(mesh.devices.reshape(rows // 2, 2, columns), ("chip", "core", "fsdp"))
    return jax.shard_map(
        on_device, mesh=split_mesh, in_specs=placed, out_specs=P(SEQ, "fsdp"), check_vma=False
    )
```

```python
import math

import jax
import jax.numpy as jnp
from jax import lax
from jax.sharding import PartitionSpec as P

KEY_VALUE_HEADS = 8
IMAGE_LOOKBACK = 4


def from_behind(value, axis, steps):
    count = lax.axis_size(axis)
    initial, last = (max(0, -steps), min(count, count - steps))
    return lax.ppermute(value, axis, [(source, source + steps) for source in range(initial, last)])


def rms_scale(values, gain):
    return values * lax.rsqrt(jnp.mean(values * values, axis=-1, keepdims=True) + 1e-05) * gain


def attend_part(grouped, key_value_pair, column_live):
    head_dim = grouped.shape[-1]
    scores = jnp.einsum(
        "kqd,knd->kqn", grouped, key_value_pair[..., :head_dim], preferred_element_type=jnp.float32
    ) * (1.0 / math.sqrt(head_dim))
    scores = jnp.where(column_live[None, None, :], scores, -jnp.inf)
    row_peak = jnp.max(scores, axis=-1, keepdims=True)
    weights = jnp.exp(scores - jnp.where(row_peak == -jnp.inf, 0.0, row_peak))
    row_total = jnp.sum(weights, axis=-1, keepdims=True)
    blended = jnp.einsum(
        "kqn,knd->kqd",
        weights.astype(jnp.bfloat16),
        key_value_pair[..., head_dim:],
        preferred_element_type=jnp.float32,
    )
    return row_peak, row_total, blended


def attend(query_heads, own, own_live, earlier, earlier_live):
    kv_heads, _, double_width = own.shape
    head_dim = double_width // 2
    row_count, heads_local, _ = query_heads.shape
    heads_per_group = heads_local // kv_heads
    grouped = query_heads.reshape(row_count, kv_heads, heads_per_group, head_dim)
    grouped = grouped.transpose(1, 2, 0, 3).reshape(kv_heads, heads_per_group * row_count, head_dim)
    own_peak, own_total, own_blend = attend_part(grouped, own, own_live)
    far_peak, far_total, far_blend = attend_part(grouped, earlier, earlier_live)
    peak = jnp.maximum(own_peak, far_peak)
    own_scale = jnp.exp(own_peak - peak)
    far_scale = jnp.exp(far_peak - peak)
    outputs = (own_blend * own_scale + far_blend * far_scale) / (
        own_total * own_scale + far_total * far_scale
    )
    outputs = outputs.reshape(kv_heads, heads_per_group, row_count, head_dim).transpose(2, 0, 1, 3)
    return outputs.reshape(row_count, heads_local * head_dim).astype(jnp.bfloat16)


def on_device(
    text_states,
    images,
    norm_gain,
    query_weight,
    image_projection_weight,
    query_gain,
    key_gain,
    admission,
):
    head_dim = query_gain.shape[0]
    local_key_value = KEY_VALUE_HEADS // lax.axis_size("fsdp")
    heads_local = query_weight.shape[1] // head_dim
    row_count = text_states.shape[0]
    normed = rms_scale(text_states.astype(jnp.float32), norm_gain).astype(jnp.bfloat16)
    kv_rows, kv_width = image_projection_weight.shape
    query_width = query_weight.shape[1]
    column_blocks = kv_width // query_width
    kv_as_rows = (
        image_projection_weight.reshape(kv_rows, column_blocks, query_width)
        .transpose(1, 0, 2)
        .reshape(column_blocks * kv_rows, query_width)
    )
    both = lax.all_gather(
        jnp.concatenate([kv_as_rows, query_weight], axis=0), "seq", axis=0, tiled=False
    )
    query_block = both[:, column_blocks * kv_rows :].reshape(-1, query_width)
    queries = jnp.dot(normed, query_block, preferred_element_type=jnp.float32)
    query_heads = rms_scale(queries.reshape(row_count, heads_local, head_dim), query_gain).astype(
        jnp.bfloat16
    )
    features = images[0]
    pair_width = 2 * head_dim
    pairs_per_block = query_width // pair_width
    partials = jnp.stack(
        [
            jnp.dot(
                features,
                both[:, block * kv_rows : (block + 1) * kv_rows, pair * pair_width : (pair + 1) * pair_width]
                .reshape(-1, pair_width),
                preferred_element_type=jnp.float32,
            ).astype(jnp.bfloat16)
            for block in range(column_blocks)
            for pair in range(pairs_per_block)
        ]
    )
    own_kv = jnp.sum(
        lax.all_to_all(partials, "fsdp", 0, 0, tiled=True).astype(jnp.float32), axis=0, keepdims=True
    )
    key_part = rms_scale(own_kv[..., :head_dim], key_gain)
    packed = jnp.concatenate([key_part, own_kv[..., head_dim:]], axis=-1).astype(jnp.bfloat16)
    span_index = lax.axis_index("seq")
    image_ids = span_index - jnp.arange(IMAGE_LOOKBACK + 1, dtype=jnp.int32)
    admitted = (image_ids >= 0) & (jnp.take(admission[0], jnp.maximum(image_ids, 0)) == 1)
    earlier_admitted = admitted[1:]
    nearest = jnp.argmax(earlier_admitted)
    farthest = IMAGE_LOOKBACK - 1 - jnp.argmax(earlier_admitted[::-1])
    admitted_count = jnp.sum(earlier_admitted.astype(jnp.int32))
    two_behind = from_behind(packed, "seq", 2)
    four_behind = from_behind(packed, "seq", 4)
    partner = lax.ppermute(
        jnp.stack([packed, two_behind, four_behind]),
        "seq",
        [(source, source ^ 1) for source in range(lax.axis_size("seq"))],
    )
    first_core = span_index % 2 == 0
    received = [
        jnp.where(first_core, partner[1], partner[0]),
        two_behind,
        jnp.where(first_core, partner[2], partner[1]),
        four_behind,
    ]

    def pick(slot):
        chosen = received[-1]
        for distance in range(IMAGE_LOOKBACK - 2, -1, -1):
            chosen = jnp.where(slot == distance, received[distance], chosen)
        return chosen

    earlier = jnp.concatenate([pick(nearest), pick(farthest)], axis=1)
    image_tokens = packed.shape[1]
    earlier_live = jnp.concatenate(
        [
            jnp.broadcast_to(admitted_count >= 1, (image_tokens,)),
            jnp.broadcast_to(admitted_count >= 2, (image_tokens,)),
        ]
    )
    own_live = jnp.broadcast_to(admitted[0], (image_tokens,))
    return attend(query_heads, packed, own_live, earlier, earlier_live)


def solution(mesh):
    placed = (
        P("seq", None),
        P("seq", None, "fsdp"),
        P(),
        P("seq", "fsdp"),
        P(("fsdp", "seq"), None),
        P(),
        P(),
        P("seq", None),
    )
    return jax.shard_map(
        on_device, mesh=mesh, in_specs=placed, out_specs=P("seq", "fsdp"), check_vma=False
    )
```

```python
import math

import jax
import jax.numpy as jnp
from jax import lax
from jax.sharding import PartitionSpec as P

KEY_VALUE_HEADS = 8
SEQ_AXIS = "seq"
IMAGE_LOOKBACK = 4


def from_behind(value, axis, steps):
    count = lax.axis_size(axis)
    initial, last = (max(0, -steps), min(count, count - steps))
    return lax.ppermute(value, axis, [(source, source + steps) for source in range(initial, last)])


def rms_scale(values, gain):
    return values * lax.rsqrt(jnp.mean(values * values, axis=-1, keepdims=True) + 1e-05) * gain


def attend_part(grouped, key_value_pair, column_live):
    head_dim = grouped.shape[-1]
    scores = jnp.einsum(
        "kqd,knd->kqn", grouped, key_value_pair[..., :head_dim], preferred_element_type=jnp.float32
    ) * (1.0 / math.sqrt(head_dim))
    scores = jnp.where(column_live[None, None, :], scores, -jnp.inf)
    row_peak = jnp.max(scores, axis=-1, keepdims=True)
    weights = jnp.exp(scores - jnp.where(row_peak == -jnp.inf, 0.0, row_peak))
    row_total = jnp.sum(weights, axis=-1, keepdims=True)
    blended = jnp.einsum(
        "kqn,knd->kqd",
        weights.astype(jnp.bfloat16),
        key_value_pair[..., head_dim:],
        preferred_element_type=jnp.float32,
    )
    return row_peak, row_total, blended


def attend(query_heads, own, own_live, earlier, earlier_live):
    kv_heads, _, double_width = own.shape
    head_dim = double_width // 2
    row_count, heads_local, _ = query_heads.shape
    heads_per_group = heads_local // kv_heads
    grouped = query_heads.reshape(row_count, kv_heads, heads_per_group, head_dim)
    grouped = grouped.transpose(1, 2, 0, 3).reshape(kv_heads, heads_per_group * row_count, head_dim)
    own_peak, own_total, own_blend = attend_part(grouped, own, own_live)
    far_peak, far_total, far_blend = attend_part(grouped, earlier, earlier_live)
    peak = jnp.maximum(own_peak, far_peak)
    own_scale = jnp.exp(own_peak - peak)
    far_scale = jnp.exp(far_peak - peak)
    outputs = (own_blend * own_scale + far_blend * far_scale) / (
        own_total * own_scale + far_total * far_scale
    )
    outputs = outputs.reshape(kv_heads, heads_per_group, row_count, head_dim).transpose(2, 0, 1, 3)
    return outputs.reshape(row_count, heads_local * head_dim).astype(jnp.bfloat16)


def on_device(
    text_states,
    images,
    norm_gain,
    query_weight,
    image_projection_weight,
    query_gain,
    key_gain,
    admission,
):
    head_dim = query_gain.shape[0]
    local_key_value = KEY_VALUE_HEADS // lax.axis_size("fsdp")
    heads_local = query_weight.shape[1] // head_dim
    row_count = text_states.shape[0]
    normed = rms_scale(text_states.astype(jnp.float32), norm_gain).astype(jnp.bfloat16)
    kv_rows, kv_width = image_projection_weight.shape
    query_width = query_weight.shape[1]
    column_blocks = kv_width // query_width
    kv_as_rows = (
        image_projection_weight.reshape(kv_rows, column_blocks, query_width)
        .transpose(1, 0, 2)
        .reshape(column_blocks * kv_rows, query_width)
    )
    both = lax.all_gather(
        jnp.concatenate([kv_as_rows, query_weight], axis=0), "seq", axis=0, tiled=False
    )
    query_block = both[:, column_blocks * kv_rows :].reshape(-1, query_width)
    queries = jnp.dot(normed, query_block, preferred_element_type=jnp.float32)
    query_heads = rms_scale(queries.reshape(row_count, heads_local, head_dim), query_gain).astype(
        jnp.bfloat16
    )
    features = images[0]
    pair_width = 2 * head_dim
    pairs_per_block = query_width // pair_width
    partials = jnp.stack(
        [
            jnp.dot(
                features,
                both[:, block * kv_rows : (block + 1) * kv_rows, pair * pair_width : (pair + 1) * pair_width]
                .reshape(-1, pair_width),
                preferred_element_type=jnp.float32,
            ).astype(jnp.bfloat16)
            for block in range(column_blocks)
            for pair in range(pairs_per_block)
        ]
    )
    own_kv = lax.psum_scatter(partials, "fsdp", scatter_dimension=0, tiled=True)

    def finish(summed):
        summed = summed.astype(jnp.float32)
        key_part = rms_scale(summed[..., :head_dim], key_gain)
        return jnp.concatenate([key_part, summed[..., head_dim:]], axis=-1).astype(jnp.bfloat16)

    span_index = lax.axis_index("seq")
    image_ids = span_index - jnp.arange(IMAGE_LOOKBACK + 1, dtype=jnp.int32)
    admitted = (image_ids >= 0) & (jnp.take(admission[0], jnp.maximum(image_ids, 0)) == 1)
    earlier_admitted = admitted[1:]
    nearest = jnp.argmax(earlier_admitted)
    farthest = IMAGE_LOOKBACK - 1 - jnp.argmax(earlier_admitted[::-1])
    admitted_count = jnp.sum(earlier_admitted.astype(jnp.int32))
    two_behind = from_behind(own_kv, SEQ_AXIS, 2)
    four_behind = from_behind(own_kv, SEQ_AXIS, 4)
    swap = [(source, source ^ 1) for source in range(lax.axis_size(SEQ_AXIS))]
    partner_own = lax.ppermute(own_kv, SEQ_AXIS, swap)
    partner_far = lax.ppermute(jnp.stack([two_behind, four_behind]), SEQ_AXIS, swap)
    first_core = span_index % 2 == 0
    received = [
        jnp.where(first_core, partner_far[0], partner_own),
        two_behind,
        jnp.where(first_core, partner_far[1], partner_far[0]),
        four_behind,
    ]

    def pick(slot):
        chosen = received[-1]
        for distance in range(IMAGE_LOOKBACK - 2, -1, -1):
            chosen = jnp.where(slot == distance, received[distance], chosen)
        return chosen

    earlier = jnp.concatenate([finish(pick(nearest)), finish(pick(farthest))], axis=1)
    packed = finish(own_kv)
    image_tokens = packed.shape[1]
    earlier_live = jnp.concatenate(
        [
            jnp.broadcast_to(admitted_count >= 1, (image_tokens,)),
            jnp.broadcast_to(admitted_count >= 2, (image_tokens,)),
        ]
    )
    own_live = jnp.broadcast_to(admitted[0], (image_tokens,))
    return attend(query_heads, packed, own_live, earlier, earlier_live)


def solution(mesh):
    placed = (
        P("seq", None),
        P("seq", None, "fsdp"),
        P(),
        P("seq", "fsdp"),
        P(("fsdp", "seq"), None),
        P(),
        P(),
        P("seq", None),
    )
    return jax.shard_map(
        on_device, mesh=mesh, in_specs=placed, out_specs=P("seq", "fsdp"), check_vma=False
    )
```

```python
import math

import jax
import jax.numpy as jnp
from jax import lax
from jax.sharding import PartitionSpec as P

KEY_VALUE_HEADS = 8
IMAGE_LOOKBACK = 4


def from_behind(value, axis, steps):
    count = lax.axis_size(axis)
    initial, last = (max(0, -steps), min(count, count - steps))
    return lax.ppermute(value, axis, [(source, source + steps) for source in range(initial, last)])


def rms_scale(values, gain):
    return values * lax.rsqrt(jnp.mean(values * values, axis=-1, keepdims=True) + 1e-05) * gain


def attend_part(grouped, key_value_pair, column_live):
    head_dim = grouped.shape[-1]
    scores = jnp.einsum(
        "kqd,knd->kqn", grouped, key_value_pair[..., :head_dim], preferred_element_type=jnp.float32
    ) * (1.0 / math.sqrt(head_dim))
    scores = jnp.where(column_live[None, None, :], scores, -jnp.inf)
    row_peak = jnp.max(scores, axis=-1, keepdims=True)
    weights = jnp.exp(scores - jnp.where(row_peak == -jnp.inf, 0.0, row_peak))
    row_total = jnp.sum(weights, axis=-1, keepdims=True)
    blended = jnp.einsum(
        "kqn,knd->kqd",
        weights.astype(jnp.bfloat16),
        key_value_pair[..., head_dim:],
        preferred_element_type=jnp.float32,
    )
    return row_peak, row_total, blended


def attend(query_heads, own, own_live, earlier, earlier_live):
    kv_heads, _, double_width = own.shape
    head_dim = double_width // 2
    row_count, heads_local, _ = query_heads.shape
    heads_per_group = heads_local // kv_heads
    grouped = query_heads.reshape(row_count, kv_heads, heads_per_group, head_dim)
    grouped = grouped.transpose(1, 2, 0, 3).reshape(kv_heads, heads_per_group * row_count, head_dim)
    own_peak, own_total, own_blend = attend_part(grouped, own, own_live)
    far_peak, far_total, far_blend = attend_part(grouped, earlier, earlier_live)
    peak = jnp.maximum(own_peak, far_peak)
    own_scale = jnp.exp(own_peak - peak)
    far_scale = jnp.exp(far_peak - peak)
    outputs = (own_blend * own_scale + far_blend * far_scale) / (
        own_total * own_scale + far_total * far_scale
    )
    outputs = outputs.reshape(kv_heads, heads_per_group, row_count, head_dim).transpose(2, 0, 1, 3)
    return outputs.reshape(row_count, heads_local * head_dim).astype(jnp.bfloat16)


def on_device(
    text_states,
    images,
    norm_gain,
    query_weight,
    image_projection_weight,
    query_gain,
    key_gain,
    admission,
):
    head_dim = query_gain.shape[0]
    local_key_value = KEY_VALUE_HEADS // lax.axis_size("fsdp")
    heads_local = query_weight.shape[1] // head_dim
    row_count = text_states.shape[0]
    normed = rms_scale(text_states.astype(jnp.float32), norm_gain).astype(jnp.bfloat16)
    kv_rows, kv_width = image_projection_weight.shape
    query_width = query_weight.shape[1]
    column_blocks = kv_width // query_width
    kv_as_rows = (
        image_projection_weight.reshape(kv_rows, column_blocks, query_width)
        .transpose(1, 0, 2)
        .reshape(column_blocks * kv_rows, query_width)
    )
    both = lax.all_gather(
        jnp.concatenate([kv_as_rows, query_weight], axis=0), "seq", axis=0, tiled=False
    )
    query_block = both[:, column_blocks * kv_rows :].reshape(-1, query_width)
    queries = jnp.dot(normed, query_block, preferred_element_type=jnp.float32)
    query_heads = rms_scale(queries.reshape(row_count, heads_local, head_dim), query_gain).astype(
        jnp.bfloat16
    )
    features = images[0]
    pair_width = 2 * head_dim
    pairs_per_block = query_width // pair_width

    def reduced_half(rows):
        partials = jnp.stack(
            [
                jnp.dot(
                    rows,
                    both[:, block * kv_rows : (block + 1) * kv_rows, pair * pair_width : (pair + 1) * pair_width]
                    .reshape(-1, pair_width),
                    preferred_element_type=jnp.float32,
                ).astype(jnp.bfloat16)
                for block in range(column_blocks)
                for pair in range(pairs_per_block)
            ]
        )
        own_kv = lax.psum_scatter(partials, "fsdp", scatter_dimension=0, tiled=True).astype(jnp.float32)
        key_part = rms_scale(own_kv[..., :head_dim], key_gain)
        return jnp.concatenate([key_part, own_kv[..., head_dim:]], axis=-1).astype(jnp.bfloat16)

    token_cut = (features.shape[0] // 16) * 8
    packed_halves = [reduced_half(features[:token_cut]), reduced_half(features[token_cut:])]
    span_index = lax.axis_index("seq")
    image_ids = span_index - jnp.arange(IMAGE_LOOKBACK + 1, dtype=jnp.int32)
    admitted = (image_ids >= 0) & (jnp.take(admission[0], jnp.maximum(image_ids, 0)) == 1)
    earlier_admitted = admitted[1:]
    nearest = jnp.argmax(earlier_admitted)
    farthest = IMAGE_LOOKBACK - 1 - jnp.argmax(earlier_admitted[::-1])
    admitted_count = jnp.sum(earlier_admitted.astype(jnp.int32))
    first_core = span_index % 2 == 0
    received_halves = []
    for half in packed_halves:
        two_behind = from_behind(half, "seq", 2)
        four_behind = from_behind(half, "seq", 4)
        partner = lax.ppermute(
            jnp.stack([half, two_behind, four_behind]),
            "seq",
            [(source, source ^ 1) for source in range(lax.axis_size("seq"))],
        )
        received_halves.append(
            [
                jnp.where(first_core, partner[1], partner[0]),
                two_behind,
                jnp.where(first_core, partner[2], partner[1]),
                four_behind,
            ]
        )
    received = [jnp.concatenate(pieces, axis=1) for pieces in zip(*received_halves)]
    packed = jnp.concatenate(packed_halves, axis=1)

    def pick(slot):
        chosen = received[-1]
        for distance in range(IMAGE_LOOKBACK - 2, -1, -1):
            chosen = jnp.where(slot == distance, received[distance], chosen)
        return chosen

    earlier = jnp.concatenate([pick(nearest), pick(farthest)], axis=1)
    image_tokens = packed.shape[1]
    earlier_live = jnp.concatenate(
        [
            jnp.broadcast_to(admitted_count >= 1, (image_tokens,)),
            jnp.broadcast_to(admitted_count >= 2, (image_tokens,)),
        ]
    )
    own_live = jnp.broadcast_to(admitted[0], (image_tokens,))
    return attend(query_heads, packed, own_live, earlier, earlier_live)


def solution(mesh):
    placed = (
        P("seq", None),
        P("seq", None, "fsdp"),
        P(),
        P("seq", "fsdp"),
        P(("fsdp", "seq"), None),
        P(),
        P(),
        P("seq", None),
    )
    return jax.shard_map(
        on_device, mesh=mesh, in_specs=placed, out_specs=P("seq", "fsdp"), check_vma=False
    )
```

```python
import math

import jax
import jax.numpy as jnp
from jax import lax
from jax.sharding import PartitionSpec as P

KEY_VALUE_HEADS = 8
IMAGE_LOOKBACK = 4


def from_behind(value, axis, steps):
    count = lax.axis_size(axis)
    initial, last = (max(0, -steps), min(count, count - steps))
    return lax.ppermute(value, axis, [(source, source + steps) for source in range(initial, last)])


def rms_scale(values, gain):
    return values * lax.rsqrt(jnp.mean(values * values, axis=-1, keepdims=True) + 1e-05) * gain


def attend_part(grouped, key_value_pair, column_live):
    head_dim = grouped.shape[-1]
    scores = jnp.einsum(
        "kqd,knd->kqn", grouped, key_value_pair[..., :head_dim], preferred_element_type=jnp.float32
    ) * (1.0 / math.sqrt(head_dim))
    scores = jnp.where(column_live[None, None, :], scores, -jnp.inf)
    row_peak = jnp.max(scores, axis=-1, keepdims=True)
    weights = jnp.exp(scores - jnp.where(row_peak == -jnp.inf, 0.0, row_peak))
    row_total = jnp.sum(weights, axis=-1, keepdims=True)
    blended = jnp.einsum(
        "kqn,knd->kqd",
        weights.astype(jnp.bfloat16),
        key_value_pair[..., head_dim:],
        preferred_element_type=jnp.float32,
    )
    return row_peak, row_total, blended


def attend(query_heads, own, own_live, earlier, earlier_live):
    kv_heads, _, double_width = own.shape
    head_dim = double_width // 2
    row_count, heads_local, _ = query_heads.shape
    heads_per_group = heads_local // kv_heads
    grouped = query_heads.reshape(row_count, kv_heads, heads_per_group, head_dim)
    grouped = grouped.transpose(1, 2, 0, 3).reshape(kv_heads, heads_per_group * row_count, head_dim)
    own_peak, own_total, own_blend = attend_part(grouped, own, own_live)
    far_peak, far_total, far_blend = attend_part(grouped, earlier, earlier_live)
    peak = jnp.maximum(own_peak, far_peak)
    own_scale = jnp.exp(own_peak - peak)
    far_scale = jnp.exp(far_peak - peak)
    outputs = (own_blend * own_scale + far_blend * far_scale) / (
        own_total * own_scale + far_total * far_scale
    )
    outputs = outputs.reshape(kv_heads, heads_per_group, row_count, head_dim).transpose(2, 0, 1, 3)
    return outputs.reshape(row_count, heads_local * head_dim).astype(jnp.bfloat16)


def on_device(
    text_states,
    images,
    norm_gain,
    query_weight,
    image_projection_weight,
    query_gain,
    key_gain,
    admission,
):
    head_dim = query_gain.shape[0]
    local_key_value = KEY_VALUE_HEADS // lax.axis_size("fsdp")
    heads_local = query_weight.shape[1] // head_dim
    row_count = text_states.shape[0]
    normed = rms_scale(text_states.astype(jnp.float32), norm_gain).astype(jnp.bfloat16)
    kv_rows, kv_width = image_projection_weight.shape
    query_width = query_weight.shape[1]
    column_blocks = kv_width // query_width
    kv_as_rows = (
        image_projection_weight.reshape(kv_rows, column_blocks, query_width)
        .transpose(1, 0, 2)
        .reshape(column_blocks * kv_rows, query_width)
    )
    both = lax.all_gather(
        jnp.concatenate([kv_as_rows, query_weight], axis=0), "seq", axis=0, tiled=False
    )
    query_block = both[:, column_blocks * kv_rows :].reshape(-1, query_width)
    queries = jnp.dot(normed, query_block, preferred_element_type=jnp.float32)
    query_heads = rms_scale(queries.reshape(row_count, heads_local, head_dim), query_gain).astype(
        jnp.bfloat16
    )
    features = images[0]
    pair_width = 2 * head_dim
    pairs_per_block = query_width // pair_width

    def reduced_half(rows):
        partials = jnp.stack(
            [
                jnp.dot(
                    rows,
                    both[:, block * kv_rows : (block + 1) * kv_rows, pair * pair_width : (pair + 1) * pair_width]
                    .reshape(-1, pair_width),
                    preferred_element_type=jnp.float32,
                ).astype(jnp.bfloat16)
                for block in range(column_blocks)
                for pair in range(pairs_per_block)
            ]
        )
        own_kv = lax.psum_scatter(partials, "fsdp", scatter_dimension=0, tiled=True).astype(jnp.float32)
        key_part = rms_scale(own_kv[..., :head_dim], key_gain)
        return jnp.concatenate([key_part, own_kv[..., head_dim:]], axis=-1).astype(jnp.bfloat16)

    token_cut = (features.shape[0] * 2 // 24) * 8
    packed_halves = [reduced_half(features[:token_cut]), reduced_half(features[token_cut:])]
    span_index = lax.axis_index("seq")
    image_ids = span_index - jnp.arange(IMAGE_LOOKBACK + 1, dtype=jnp.int32)
    admitted = (image_ids >= 0) & (jnp.take(admission[0], jnp.maximum(image_ids, 0)) == 1)
    earlier_admitted = admitted[1:]
    nearest = jnp.argmax(earlier_admitted)
    farthest = IMAGE_LOOKBACK - 1 - jnp.argmax(earlier_admitted[::-1])
    admitted_count = jnp.sum(earlier_admitted.astype(jnp.int32))
    first_core = span_index % 2 == 0
    received_halves = []
    for half in packed_halves:
        two_behind = from_behind(half, "seq", 2)
        four_behind = from_behind(half, "seq", 4)
        partner = lax.ppermute(
            jnp.stack([half, two_behind, four_behind]),
            "seq",
            [(source, source ^ 1) for source in range(lax.axis_size("seq"))],
        )
        received_halves.append(
            [
                jnp.where(first_core, partner[1], partner[0]),
                two_behind,
                jnp.where(first_core, partner[2], partner[1]),
                four_behind,
            ]
        )
    received = [jnp.concatenate(pieces, axis=1) for pieces in zip(*received_halves)]
    packed = jnp.concatenate(packed_halves, axis=1)

    def pick(slot):
        chosen = received[-1]
        for distance in range(IMAGE_LOOKBACK - 2, -1, -1):
            chosen = jnp.where(slot == distance, received[distance], chosen)
        return chosen

    earlier = jnp.concatenate([pick(nearest), pick(farthest)], axis=1)
    image_tokens = packed.shape[1]
    earlier_live = jnp.concatenate(
        [
            jnp.broadcast_to(admitted_count >= 1, (image_tokens,)),
            jnp.broadcast_to(admitted_count >= 2, (image_tokens,)),
        ]
    )
    own_live = jnp.broadcast_to(admitted[0], (image_tokens,))
    return attend(query_heads, packed, own_live, earlier, earlier_live)


def solution(mesh):
    placed = (
        P("seq", None),
        P("seq", None, "fsdp"),
        P(),
        P("seq", "fsdp"),
        P(("fsdp", "seq"), None),
        P(),
        P(),
        P("seq", None),
    )
    return jax.shard_map(
        on_device, mesh=mesh, in_specs=placed, out_specs=P("seq", "fsdp"), check_vma=False
    )
```

```python
import math

import jax
import jax.numpy as jnp
from jax import lax
from jax.sharding import PartitionSpec as P

KEY_VALUE_HEADS = 8
IMAGE_LOOKBACK = 4


def from_behind(value, axis, steps):
    count = lax.axis_size(axis)
    initial, last = (max(0, -steps), min(count, count - steps))
    return lax.ppermute(value, axis, [(source, source + steps) for source in range(initial, last)])


def rms_scale(values, gain):
    return values * lax.rsqrt(jnp.mean(values * values, axis=-1, keepdims=True) + 1e-05) * gain


def attend_part(grouped, key_value_pair, column_live):
    head_dim = grouped.shape[-1]
    scores = jnp.einsum(
        "kqd,knd->kqn", grouped, key_value_pair[..., :head_dim], preferred_element_type=jnp.float32
    ) * (1.0 / math.sqrt(head_dim))
    scores = jnp.where(column_live[None, None, :], scores, -jnp.inf)
    row_peak = jnp.max(scores, axis=-1, keepdims=True)
    weights = jnp.exp(scores - jnp.where(row_peak == -jnp.inf, 0.0, row_peak))
    row_total = jnp.sum(weights, axis=-1, keepdims=True)
    blended = jnp.einsum(
        "kqn,knd->kqd",
        weights.astype(jnp.bfloat16),
        key_value_pair[..., head_dim:],
        preferred_element_type=jnp.float32,
    )
    return row_peak, row_total, blended


def attend(query_heads, own, own_live, earlier, earlier_live):
    kv_heads, _, double_width = own.shape
    head_dim = double_width // 2
    row_count, heads_local, _ = query_heads.shape
    heads_per_group = heads_local // kv_heads
    grouped = query_heads.reshape(row_count, kv_heads, heads_per_group, head_dim)
    grouped = grouped.transpose(1, 2, 0, 3).reshape(kv_heads, heads_per_group * row_count, head_dim)
    own_peak, own_total, own_blend = attend_part(grouped, own, own_live)
    far_peak, far_total, far_blend = attend_part(grouped, earlier, earlier_live)
    peak = jnp.maximum(own_peak, far_peak)
    own_scale = jnp.exp(own_peak - peak)
    far_scale = jnp.exp(far_peak - peak)
    outputs = (own_blend * own_scale + far_blend * far_scale) / (
        own_total * own_scale + far_total * far_scale
    )
    outputs = outputs.reshape(kv_heads, heads_per_group, row_count, head_dim).transpose(2, 0, 1, 3)
    return outputs.reshape(row_count, heads_local * head_dim).astype(jnp.bfloat16)


def on_device(
    text_states,
    images,
    norm_gain,
    query_weight,
    image_projection_weight,
    query_gain,
    key_gain,
    admission,
):
    head_dim = query_gain.shape[0]
    local_key_value = KEY_VALUE_HEADS // lax.axis_size("fsdp")
    heads_local = query_weight.shape[1] // head_dim
    row_count = text_states.shape[0]
    normed = rms_scale(text_states.astype(jnp.float32), norm_gain).astype(jnp.bfloat16)
    kv_rows, kv_width = image_projection_weight.shape
    query_width = query_weight.shape[1]
    column_blocks = kv_width // query_width
    kv_as_rows = (
        image_projection_weight.reshape(kv_rows, column_blocks, query_width)
        .transpose(1, 0, 2)
        .reshape(column_blocks * kv_rows, query_width)
    )
    both = lax.all_gather(
        jnp.concatenate([kv_as_rows, query_weight], axis=0), "seq", axis=0, tiled=False
    )
    query_block = both[:, column_blocks * kv_rows :].reshape(-1, query_width)
    queries = jnp.dot(normed, query_block, preferred_element_type=jnp.float32)
    query_heads = rms_scale(queries.reshape(row_count, heads_local, head_dim), query_gain).astype(
        jnp.bfloat16
    )
    features = images[0]
    pair_width = 2 * head_dim
    pairs_per_block = query_width // pair_width

    def reduced_half(rows):
        partials = jnp.stack(
            [
                jnp.dot(
                    rows,
                    both[:, block * kv_rows : (block + 1) * kv_rows, pair * pair_width : (pair + 1) * pair_width]
                    .reshape(-1, pair_width),
                    preferred_element_type=jnp.float32,
                ).astype(jnp.bfloat16)
                for block in range(column_blocks)
                for pair in range(pairs_per_block)
            ]
        )
        own_kv = jnp.sum(
            lax.all_to_all(partials, "fsdp", 0, 0, tiled=True).astype(jnp.float32), axis=0, keepdims=True
        )
        key_part = rms_scale(own_kv[..., :head_dim], key_gain)
        return jnp.concatenate([key_part, own_kv[..., head_dim:]], axis=-1).astype(jnp.bfloat16)

    token_cut = (features.shape[0] // 16) * 8
    packed_halves = [reduced_half(features[:token_cut]), reduced_half(features[token_cut:])]
    span_index = lax.axis_index("seq")
    image_ids = span_index - jnp.arange(IMAGE_LOOKBACK + 1, dtype=jnp.int32)
    admitted = (image_ids >= 0) & (jnp.take(admission[0], jnp.maximum(image_ids, 0)) == 1)
    earlier_admitted = admitted[1:]
    nearest = jnp.argmax(earlier_admitted)
    farthest = IMAGE_LOOKBACK - 1 - jnp.argmax(earlier_admitted[::-1])
    admitted_count = jnp.sum(earlier_admitted.astype(jnp.int32))
    first_core = span_index % 2 == 0
    received_halves = []
    for half in packed_halves:
        two_behind = from_behind(half, "seq", 2)
        four_behind = from_behind(half, "seq", 4)
        partner = lax.ppermute(
            jnp.stack([half, two_behind, four_behind]),
            "seq",
            [(source, source ^ 1) for source in range(lax.axis_size("seq"))],
        )
        received_halves.append(
            [
                jnp.where(first_core, partner[1], partner[0]),
                two_behind,
                jnp.where(first_core, partner[2], partner[1]),
                four_behind,
            ]
        )
    received = [jnp.concatenate(pieces, axis=1) for pieces in zip(*received_halves)]
    packed = jnp.concatenate(packed_halves, axis=1)

    def pick(slot):
        chosen = received[-1]
        for distance in range(IMAGE_LOOKBACK - 2, -1, -1):
            chosen = jnp.where(slot == distance, received[distance], chosen)
        return chosen

    earlier = jnp.concatenate([pick(nearest), pick(farthest)], axis=1)
    image_tokens = packed.shape[1]
    earlier_live = jnp.concatenate(
        [
            jnp.broadcast_to(admitted_count >= 1, (image_tokens,)),
            jnp.broadcast_to(admitted_count >= 2, (image_tokens,)),
        ]
    )
    own_live = jnp.broadcast_to(admitted[0], (image_tokens,))
    return attend(query_heads, packed, own_live, earlier, earlier_live)


def solution(mesh):
    placed = (
        P("seq", None),
        P("seq", None, "fsdp"),
        P(),
        P("seq", "fsdp"),
        P(("fsdp", "seq"), None),
        P(),
        P(),
        P("seq", None),
    )
    return jax.shard_map(
        on_device, mesh=mesh, in_specs=placed, out_specs=P("seq", "fsdp"), check_vma=False
    )
```

```python
import math

import jax
import jax.numpy as jnp
from jax import lax
from jax.sharding import PartitionSpec as P

KEY_VALUE_HEADS = 8
IMAGE_LOOKBACK = 4


def from_behind(value, axis, steps):
    count = lax.axis_size(axis)
    initial, last = (max(0, -steps), min(count, count - steps))
    return lax.ppermute(value, axis, [(source, source + steps) for source in range(initial, last)])


def rms_scale(values, gain):
    return values * lax.rsqrt(jnp.mean(values * values, axis=-1, keepdims=True) + 1e-05) * gain


def attend_part(grouped, key_value_pair, column_live):
    head_dim = grouped.shape[-1]
    scores = jnp.einsum(
        "kqd,knd->kqn", grouped, key_value_pair[..., :head_dim], preferred_element_type=jnp.float32
    ) * (1.0 / math.sqrt(head_dim))
    scores = jnp.where(column_live[None, None, :], scores, -jnp.inf)
    row_peak = jnp.max(scores, axis=-1, keepdims=True)
    weights = jnp.exp(scores - jnp.where(row_peak == -jnp.inf, 0.0, row_peak))
    row_total = jnp.sum(weights, axis=-1, keepdims=True)
    blended = jnp.einsum(
        "kqn,knd->kqd",
        weights.astype(jnp.bfloat16),
        key_value_pair[..., head_dim:],
        preferred_element_type=jnp.float32,
    )
    return row_peak, row_total, blended


def attend(query_heads, own, own_live, earlier, earlier_live):
    kv_heads, _, double_width = own.shape
    head_dim = double_width // 2
    row_count, heads_local, _ = query_heads.shape
    heads_per_group = heads_local // kv_heads
    grouped = query_heads.reshape(row_count, kv_heads, heads_per_group, head_dim)
    grouped = grouped.transpose(1, 2, 0, 3).reshape(kv_heads, heads_per_group * row_count, head_dim)
    own_peak, own_total, own_blend = attend_part(grouped, own, own_live)
    far_peak, far_total, far_blend = attend_part(grouped, earlier, earlier_live)
    peak = jnp.maximum(own_peak, far_peak)
    own_scale = jnp.exp(own_peak - peak)
    far_scale = jnp.exp(far_peak - peak)
    outputs = (own_blend * own_scale + far_blend * far_scale) / (
        own_total * own_scale + far_total * far_scale
    )
    outputs = outputs.reshape(kv_heads, heads_per_group, row_count, head_dim).transpose(2, 0, 1, 3)
    return outputs.reshape(row_count, heads_local * head_dim).astype(jnp.bfloat16)


def on_device(
    text_states,
    images,
    norm_gain,
    query_weight,
    image_projection_weight,
    query_gain,
    key_gain,
    admission,
):
    head_dim = query_gain.shape[0]
    local_key_value = KEY_VALUE_HEADS // lax.axis_size("fsdp")
    heads_local = query_weight.shape[1] // head_dim
    row_count = text_states.shape[0]
    normed = rms_scale(text_states.astype(jnp.float32), norm_gain).astype(jnp.bfloat16)
    kv_rows, kv_width = image_projection_weight.shape
    query_width = query_weight.shape[1]
    column_blocks = kv_width // query_width
    kv_as_rows = (
        image_projection_weight.reshape(kv_rows, column_blocks, query_width)
        .transpose(1, 0, 2)
        .reshape(column_blocks * kv_rows, query_width)
    )
    both = lax.all_gather(
        jnp.concatenate([kv_as_rows, query_weight], axis=0), "seq", axis=0, tiled=False
    )
    query_block = both[:, column_blocks * kv_rows :].reshape(-1, query_width)
    queries = jnp.dot(normed, query_block, preferred_element_type=jnp.float32)
    query_heads = rms_scale(queries.reshape(row_count, heads_local, head_dim), query_gain).astype(
        jnp.bfloat16
    )
    features = images[0]
    pair_width = 2 * head_dim
    pairs_per_block = query_width // pair_width

    def reduced_half(rows):
        partials = jnp.stack(
            [
                jnp.dot(
                    rows,
                    both[:, block * kv_rows : (block + 1) * kv_rows, pair * pair_width : (pair + 1) * pair_width]
                    .reshape(-1, pair_width),
                    preferred_element_type=jnp.float32,
                ).astype(jnp.bfloat16)
                for block in range(column_blocks)
                for pair in range(pairs_per_block)
            ]
        )
        own_kv = lax.psum_scatter(partials, "fsdp", scatter_dimension=0, tiled=True).astype(jnp.float32)
        key_part = rms_scale(own_kv[..., :head_dim], key_gain)
        return jnp.concatenate([key_part, own_kv[..., head_dim:]], axis=-1).astype(jnp.bfloat16)

    token_cut = (features.shape[0] // 24) * 8
    packed_halves = [
        reduced_half(features[:token_cut]),
        reduced_half(features[token_cut : 2 * token_cut]),
        reduced_half(features[2 * token_cut :]),
    ]
    span_index = lax.axis_index("seq")
    image_ids = span_index - jnp.arange(IMAGE_LOOKBACK + 1, dtype=jnp.int32)
    admitted = (image_ids >= 0) & (jnp.take(admission[0], jnp.maximum(image_ids, 0)) == 1)
    earlier_admitted = admitted[1:]
    nearest = jnp.argmax(earlier_admitted)
    farthest = IMAGE_LOOKBACK - 1 - jnp.argmax(earlier_admitted[::-1])
    admitted_count = jnp.sum(earlier_admitted.astype(jnp.int32))
    first_core = span_index % 2 == 0
    received_halves = []
    for half in packed_halves:
        two_behind = from_behind(half, "seq", 2)
        four_behind = from_behind(half, "seq", 4)
        partner = lax.ppermute(
            jnp.stack([half, two_behind, four_behind]),
            "seq",
            [(source, source ^ 1) for source in range(lax.axis_size("seq"))],
        )
        received_halves.append(
            [
                jnp.where(first_core, partner[1], partner[0]),
                two_behind,
                jnp.where(first_core, partner[2], partner[1]),
                four_behind,
            ]
        )
    received = [jnp.concatenate(pieces, axis=1) for pieces in zip(*received_halves)]
    packed = jnp.concatenate(packed_halves, axis=1)

    def pick(slot):
        chosen = received[-1]
        for distance in range(IMAGE_LOOKBACK - 2, -1, -1):
            chosen = jnp.where(slot == distance, received[distance], chosen)
        return chosen

    earlier = jnp.concatenate([pick(nearest), pick(farthest)], axis=1)
    image_tokens = packed.shape[1]
    earlier_live = jnp.concatenate(
        [
            jnp.broadcast_to(admitted_count >= 1, (image_tokens,)),
            jnp.broadcast_to(admitted_count >= 2, (image_tokens,)),
        ]
    )
    own_live = jnp.broadcast_to(admitted[0], (image_tokens,))
    return attend(query_heads, packed, own_live, earlier, earlier_live)


def solution(mesh):
    placed = (
        P("seq", None),
        P("seq", None, "fsdp"),
        P(),
        P("seq", "fsdp"),
        P(("fsdp", "seq"), None),
        P(),
        P(),
        P("seq", None),
    )
    return jax.shard_map(
        on_device, mesh=mesh, in_specs=placed, out_specs=P("seq", "fsdp"), check_vma=False
    )
```

```python
import math

import jax
import jax.numpy as jnp
from jax import lax
from jax.sharding import PartitionSpec as P

KEY_VALUE_HEADS = 8
IMAGE_LOOKBACK = 4


def from_behind(value, axis, steps):
    count = lax.axis_size(axis)
    initial, last = (max(0, -steps), min(count, count - steps))
    return lax.ppermute(value, axis, [(source, source + steps) for source in range(initial, last)])


def rms_scale(values, gain):
    return values * lax.rsqrt(jnp.mean(values * values, axis=-1, keepdims=True) + 1e-05) * gain


def attend_part(grouped, key_value_pair, column_live):
    head_dim = grouped.shape[-1]
    scores = jnp.einsum(
        "kqd,knd->kqn", grouped, key_value_pair[..., :head_dim], preferred_element_type=jnp.float32
    ) * (1.0 / math.sqrt(head_dim))
    scores = jnp.where(column_live[None, None, :], scores, -jnp.inf)
    row_peak = jnp.max(scores, axis=-1, keepdims=True)
    weights = jnp.exp(scores - jnp.where(row_peak == -jnp.inf, 0.0, row_peak))
    row_total = jnp.sum(weights, axis=-1, keepdims=True)
    blended = jnp.einsum(
        "kqn,knd->kqd",
        weights.astype(jnp.bfloat16),
        key_value_pair[..., head_dim:],
        preferred_element_type=jnp.float32,
    )
    return row_peak, row_total, blended


def attend(query_heads, own, own_live, earlier, earlier_live):
    kv_heads, _, double_width = own.shape
    head_dim = double_width // 2
    row_count, heads_local, _ = query_heads.shape
    heads_per_group = heads_local // kv_heads
    grouped = query_heads.reshape(row_count, kv_heads, heads_per_group, head_dim)
    grouped = grouped.transpose(1, 2, 0, 3).reshape(kv_heads, heads_per_group * row_count, head_dim)
    own_peak, own_total, own_blend = attend_part(grouped, own, own_live)
    far_peak, far_total, far_blend = attend_part(grouped, earlier, earlier_live)
    peak = jnp.maximum(own_peak, far_peak)
    own_scale = jnp.exp(own_peak - peak)
    far_scale = jnp.exp(far_peak - peak)
    outputs = (own_blend * own_scale + far_blend * far_scale) / (
        own_total * own_scale + far_total * far_scale
    )
    outputs = outputs.reshape(kv_heads, heads_per_group, row_count, head_dim).transpose(2, 0, 1, 3)
    return outputs.reshape(row_count, heads_local * head_dim).astype(jnp.bfloat16)


def on_device(
    text_states,
    images,
    norm_gain,
    query_weight,
    image_projection_weight,
    query_gain,
    key_gain,
    admission,
):
    head_dim = query_gain.shape[0]
    local_key_value = KEY_VALUE_HEADS // lax.axis_size("fsdp")
    heads_local = query_weight.shape[1] // head_dim
    row_count = text_states.shape[0]
    normed = rms_scale(text_states.astype(jnp.float32), norm_gain).astype(jnp.bfloat16)
    kv_rows, kv_width = image_projection_weight.shape
    query_width = query_weight.shape[1]
    column_blocks = kv_width // query_width
    kv_as_rows = (
        image_projection_weight.reshape(kv_rows, column_blocks, query_width)
        .transpose(1, 0, 2)
        .reshape(column_blocks * kv_rows, query_width)
    )
    both = lax.all_gather(
        jnp.concatenate([kv_as_rows, query_weight], axis=0), "seq", axis=0, tiled=False
    )
    query_block = both[:, column_blocks * kv_rows :].reshape(-1, query_width)
    queries = jnp.dot(normed, query_block, preferred_element_type=jnp.float32)
    query_heads = rms_scale(queries.reshape(row_count, heads_local, head_dim), query_gain).astype(
        jnp.bfloat16
    )
    features = images[0]
    pair_width = 2 * head_dim
    pairs_per_block = query_width // pair_width

    def reduced_half(rows):
        partials = jnp.stack(
            [
                jnp.dot(
                    rows,
                    both[:, block * kv_rows : (block + 1) * kv_rows, pair * pair_width : (pair + 1) * pair_width]
                    .reshape(-1, pair_width),
                    preferred_element_type=jnp.float32,
                ).astype(jnp.bfloat16)
                for block in range(column_blocks)
                for pair in range(pairs_per_block)
            ]
        )
        own_kv = lax.psum_scatter(partials, "fsdp", scatter_dimension=0, tiled=True).astype(jnp.float32)
        key_part = rms_scale(own_kv[..., :head_dim], key_gain)
        return jnp.concatenate([key_part, own_kv[..., head_dim:]], axis=-1).astype(jnp.bfloat16)

    token_cut = (features.shape[0] // 24) * 8
    packed_halves = [reduced_half(features[:token_cut]), reduced_half(features[token_cut:])]
    span_index = lax.axis_index("seq")
    image_ids = span_index - jnp.arange(IMAGE_LOOKBACK + 1, dtype=jnp.int32)
    admitted = (image_ids >= 0) & (jnp.take(admission[0], jnp.maximum(image_ids, 0)) == 1)
    earlier_admitted = admitted[1:]
    nearest = jnp.argmax(earlier_admitted)
    farthest = IMAGE_LOOKBACK - 1 - jnp.argmax(earlier_admitted[::-1])
    admitted_count = jnp.sum(earlier_admitted.astype(jnp.int32))
    first_core = span_index % 2 == 0
    received_halves = []
    for half in packed_halves:
        two_behind = from_behind(half, "seq", 2)
        four_behind = from_behind(half, "seq", 4)
        partner = lax.ppermute(
            jnp.stack([half, two_behind, four_behind]),
            "seq",
            [(source, source ^ 1) for source in range(lax.axis_size("seq"))],
        )
        received_halves.append(
            [
                jnp.where(first_core, partner[1], partner[0]),
                two_behind,
                jnp.where(first_core, partner[2], partner[1]),
                four_behind,
            ]
        )
    received = [jnp.concatenate(pieces, axis=1) for pieces in zip(*received_halves)]
    packed = jnp.concatenate(packed_halves, axis=1)

    def pick(slot):
        chosen = received[-1]
        for distance in range(IMAGE_LOOKBACK - 2, -1, -1):
            chosen = jnp.where(slot == distance, received[distance], chosen)
        return chosen

    earlier = jnp.concatenate([pick(nearest), pick(farthest)], axis=1)
    image_tokens = packed.shape[1]
    earlier_live = jnp.concatenate(
        [
            jnp.broadcast_to(admitted_count >= 1, (image_tokens,)),
            jnp.broadcast_to(admitted_count >= 2, (image_tokens,)),
        ]
    )
    own_live = jnp.broadcast_to(admitted[0], (image_tokens,))
    return attend(query_heads, packed, own_live, earlier, earlier_live)


def solution(mesh):
    placed = (
        P("seq", None),
        P("seq", None, "fsdp"),
        P(),
        P("seq", "fsdp"),
        P(("fsdp", "seq"), None),
        P(),
        P(),
        P("seq", None),
    )
    return jax.shard_map(
        on_device, mesh=mesh, in_specs=placed, out_specs=P("seq", "fsdp"), check_vma=False
    )
```
